512 devices in a mesh: dp: 8 (over z), cent: 64 (over x, y, core).
Axes of the slice: x: 4, y: 8, z: 8, core: 2. Of those that a mesh axis runs over, the one named last changes fastest.
Arguments:
- points: bfloat16 [24576, 1024], P(('dp', 'cent')), may hold values from -6 to 6
- assign: int32 [24576], P(('dp', 'cent')), may hold values from 0 to 32767, as said below
- centroids: float32 [32768, 1024], P('cent'), may hold values from -6 to 6
- counts: int32 [32768], P('cent'), may hold values from 1 to 4
Outputs:
- new_centroids: float32 [32768, 1024], P('cent')
- best: float32 [24576], P(('dp', 'cent'))
The draws below stay inside these ranges and needn't reach their ends.
Inputs may be any that keep to these rules, and one draw needn't show every extreme that they name: `assign`: split the points into aligned blocks of 3072 points in order (the points of one dp index). In every block, the clusters k * 512 to (k + 1) * 512 - 1 receive exactly 48 points together, for every k.
All inputs are finite; a program needn't handle non-finite values.
Results may differ from the reference program's by a relative error of at most 0.0003.
Values may be sent and summed in bfloat16 or wider, within the bound.
No kernel may reach another device: no remote copies, remote signals or barrier semaphores. Data moves between devices by JAX's collectives and lax.ppermute only.
A program may use at most 128 MiB of HBM per device.

```python
import jax
import jax.numpy as jnp
from jax import lax

D = 1024
K_DEV = 512
P_DEV = 48
K = 32768
N = 24576
N_CENT = 64


def draw_assign(key, part):
    shards = K // K_DEV
    group = P_DEV * shards
    blocks = N // group
    keys = jax.random.split(jax.random.fold_in(key, 17), blocks)

    def one_block(block_key):
        first, second = jax.random.split(block_key)
        order = jax.random.permutation(first, group).astype(jnp.int32)
        shard = order % shards
        within = jax.random.randint(second, (group,), 0, K_DEV, dtype=jnp.int32)
        return shard * K_DEV + within
    return jax.vmap(one_block)(keys).reshape(N).astype(jnp.int32)


def place_ends(drawn, key, low, high):
    dims = drawn.shape
    index_at = [jax.random.randint(jax.random.fold_in(key, axis), (), 0, dims[axis]) for axis in range(len(dims))]
    drawn = drawn.at[tuple(index_at)].set(low)
    longest = dims.index(max(dims))
    index_at[longest] = (index_at[longest] + 1) % dims[longest]
    return drawn.at[tuple(index_at)].set(high)


def level_of(key, extent, cuts, least, top_value):
    def one(axis_at, parts):
        draws = jax.random.uniform(jax.random.fold_in(jax.random.fold_in(key, 6), axis_at), (parts,), jnp.float32, least / len(cuts), top_value / len(cuts))
        return jnp.repeat(jnp.exp(draws), extent[axis_at] // parts).reshape((-1,) + (1,) * (len(extent) - axis_at - 1))

    factor_of = one(*cuts[0])
    for cut in cuts[1:]:
        factor_of = factor_of * one(*cut)
    return factor_of


def scatter_about(rng, extent, width, most, pieces=(), kind=jnp.bfloat16):
    level = level_of(rng, extent, pieces, -0.22, 0.18) if pieces else 1.0
    entries = jax.random.normal(rng, extent, jnp.float32) * width * level
    return jnp.minimum(jnp.maximum(entries, -most), most).astype(kind)


def setup_inputs(seed: int = 0) -> dict:
    key_of = jax.random.split(jax.random.key(seed), 5)
    return {
        "points": scatter_about(key_of[0], (N, D), 1.0, 6.0, ((0, 512),)),
        "assign": draw_assign(jax.random.fold_in(key_of[4], 71), 0),
        "centroids": scatter_about(key_of[2], (K, D), 1.0, 6.0, ((0, 64),), jnp.float32),
        "counts": place_ends(jax.random.randint(key_of[3], (K,), 1, 5), jax.random.fold_in(key_of[3], 1), 1, 4).astype(jnp.int32),
    }


def reference(points, assign, centroids, counts):
    values = points.astype(jnp.float32)
    sums = jax.ops.segment_sum(values, assign, num_segments=K_DEV * N_CENT)
    merged = centroids * counts.astype(jnp.float32)[:, None] + sums
    fresh = merged * lax.rsqrt(lax.optimization_barrier(jnp.mean(merged * merged, axis=1, keepdims=True)) + 1e-05)
    rounded = lax.optimization_barrier(fresh.astype(jnp.bfloat16)).astype(jnp.float32)
    blocks = rounded.reshape(N_CENT, K_DEV, D)

    def block_best(block):
        return lax.optimization_barrier(jnp.max(jnp.dot(values, block.T, preferred_element_type=jnp.float32), axis=1))
    top = lax.optimization_barrier(jnp.max(lax.map(block_best, blocks), axis=0))
    scale = D * jnp.sqrt(lax.optimization_barrier(jnp.mean(values * values, axis=1)) + 1e-06)
    return (fresh, top / scale)
```

```python
import jax
import jax.numpy as jnp
from jax import lax
from jax.sharding import PartitionSpec as P


def renorm(merged):
    return merged * lax.rsqrt(jnp.mean(merged * merged, axis=1, keepdims=True) + 1e-05)


def make_per_device(ncent):
    def per_device(points, assign, centroids, counts):
        kdev = centroids.shape[0]
        pdev, width = points.shape
        first = lax.axis_index("cent") * kdev
        weighted = centroids * counts.astype(jnp.float32)[:, None]

        rows = lax.all_gather(points, "cent", axis=0, tiled=True)
        labels = lax.all_to_all(
            jnp.broadcast_to(assign[None], (ncent, pdev)), "cent", 0, 0, tiled=True
        ).reshape(-1)

        local = labels - first
        mine = (local >= 0) & (local < kdev)
        rank = jnp.cumsum(mine.astype(jnp.int32)) - 1
        pick = mine[None, :] & (rank[None, :] == jnp.arange(pdev, dtype=jnp.int32)[:, None])
        picked = jnp.dot(pick.astype(jnp.bfloat16), rows, preferred_element_type=jnp.float32)
        picked_label = jnp.sum(jnp.where(pick, local[None, :], 0), axis=1)
        hi = (picked_label // 16).astype(jnp.bfloat16)
        lo = (picked_label % 16).astype(jnp.bfloat16)
        packed = jnp.concatenate(
            [picked.astype(jnp.bfloat16), hi[:, None], lo[:, None], jnp.zeros((pdev, 126), jnp.bfloat16)],
            axis=1,
        )

        gathered = lax.all_gather(packed, "dp", axis=0, tiled=True)
        grows = gathered[:, :width]
        glabel = gathered[:, width].astype(jnp.int32) * 16 + gathered[:, width + 1].astype(jnp.int32)
        onehot = (glabel[None, :] == jnp.arange(kdev, dtype=jnp.int32)[:, None]).astype(jnp.bfloat16)
        total = jnp.dot(onehot, grows, preferred_element_type=jnp.float32)

        fresh = renorm(weighted + total)
        rounded = fresh.astype(jnp.bfloat16)
        scores = jnp.dot(rows, rounded.T, preferred_element_type=jnp.float32)
        local_best = jnp.max(scores, axis=1)
        top = jnp.max(lax.all_to_all(local_best.reshape(ncent, pdev), "cent", 0, 0, tiled=True), axis=0)
        values = points.astype(jnp.float32)
        scale = width * jnp.sqrt(jnp.mean(values * values, axis=1) + 1e-06)
        return (fresh, top / scale)

    return per_device


def solution(mesh):
    placed = (P(("dp", "cent"), None), P(("dp", "cent")), P("cent", None), P("cent"))
    return jax.shard_map(
        make_per_device(mesh.shape["cent"]),
        mesh=mesh,
        in_specs=placed,
        out_specs=(P("cent", None), P(("dp", "cent"))),
        check_vma=False,
    )
```

```python
import jax
import jax.numpy as jnp
from jax import lax
from jax.sharding import PartitionSpec as P


def renorm(merged):
    return merged * lax.rsqrt(jnp.mean(merged * merged, axis=1, keepdims=True) + 1e-05)


def make_per_device(ncent):
    def per_device(points, assign, centroids, counts):
        kdev = centroids.shape[0]
        pdev, width = points.shape
        first = lax.axis_index("cent") * kdev
        weighted = centroids * counts.astype(jnp.float32)[:, None]

        rows = lax.all_gather(points, "cent", axis=0, tiled=True)
        labels = lax.all_to_all(
            jnp.broadcast_to(assign[None], (ncent, pdev)), "cent", 0, 0, tiled=True
        ).reshape(-1)

        local = labels - first
        mine = (local >= 0) & (local < kdev)
        rank = jnp.cumsum(mine.astype(jnp.int32)) - 1
        pick = mine[None, :] & (rank[None, :] == jnp.arange(pdev, dtype=jnp.int32)[:, None])
        where = jnp.sum(jnp.where(pick, jnp.arange(rows.shape[0], dtype=jnp.int32)[None, :], 0), axis=1)
        picked = jnp.take(rows, where, axis=0)
        picked_label = jnp.take(local, where, axis=0)
        hi = (picked_label // 16).astype(jnp.bfloat16)
        lo = (picked_label % 16).astype(jnp.bfloat16)
        packed = jnp.concatenate(
            [picked.astype(jnp.bfloat16), hi[:, None], lo[:, None], jnp.zeros((pdev, 126), jnp.bfloat16)],
            axis=1,
        )

        gathered = lax.all_gather(packed, "dp", axis=0, tiled=True)
        grows = gathered[:, :width]
        glabel = gathered[:, width].astype(jnp.int32) * 16 + gathered[:, width + 1].astype(jnp.int32)
        onehot = (glabel[None, :] == jnp.arange(kdev, dtype=jnp.int32)[:, None]).astype(jnp.bfloat16)
        total = jnp.dot(onehot, grows, preferred_element_type=jnp.float32)

        fresh = renorm(weighted + total)
        rounded = fresh.astype(jnp.bfloat16)
        scores = jnp.dot(rows, rounded.T, preferred_element_type=jnp.float32)
        local_best = jnp.max(scores, axis=1)
        top = jnp.max(lax.all_to_all(local_best.reshape(ncent, pdev), "cent", 0, 0, tiled=True), axis=0)
        values = points.astype(jnp.float32)
        scale = width * jnp.sqrt(jnp.mean(values * values, axis=1) + 1e-06)
        return (fresh, top / scale)

    return per_device


def solution(mesh):
    placed = (P(("dp", "cent"), None), P(("dp", "cent")), P("cent", None), P("cent"))
    return jax.shard_map(
        make_per_device(mesh.shape["cent"]),
        mesh=mesh,
        in_specs=placed,
        out_specs=(P("cent", None), P(("dp", "cent"))),
        check_vma=False,
    )
```

```python
import jax
import jax.numpy as jnp
from jax import lax
from jax.sharding import PartitionSpec as P


def renorm(merged):
    return merged * lax.rsqrt(jnp.mean(merged * merged, axis=1, keepdims=True) + 1e-05)


def make_per_device(ncent):
    def per_device(points, assign, centroids, counts):
        kdev = centroids.shape[0]
        pdev, width = points.shape
        first = lax.axis_index("cent") * kdev
        weighted = centroids * counts.astype(jnp.float32)[:, None]

        rows = lax.all_gather(points, "cent", axis=0, tiled=True)
        labels = lax.all_to_all(
            jnp.broadcast_to(assign[None], (ncent, pdev)), "cent", 0, 0, tiled=True
        ).reshape(-1)

        local = labels - first
        mine = (local >= 0) & (local < kdev)
        rank = jnp.cumsum(mine.astype(jnp.int32)) - 1
        pick = mine[None, :] & (rank[None, :] == jnp.arange(pdev, dtype=jnp.int32)[:, None])
        where = jnp.sum(jnp.where(pick, jnp.arange(rows.shape[0], dtype=jnp.int32)[None, :], 0), axis=1)
        picked = jnp.concatenate([lax.dynamic_slice_in_dim(rows, where[r], 1, 0) for r in range(pdev)], axis=0)
        picked_label = jnp.take(local, where, axis=0)
        hi = (picked_label // 16).astype(jnp.bfloat16)
        lo = (picked_label % 16).astype(jnp.bfloat16)
        packed = jnp.concatenate(
            [picked.astype(jnp.bfloat16), hi[:, None], lo[:, None], jnp.zeros((pdev, 126), jnp.bfloat16)],
            axis=1,
        )

        gathered = lax.all_gather(packed, "dp", axis=0, tiled=True)
        grows = gathered[:, :width]
        glabel = gathered[:, width].astype(jnp.int32) * 16 + gathered[:, width + 1].astype(jnp.int32)
        onehot = (glabel[None, :] == jnp.arange(kdev, dtype=jnp.int32)[:, None]).astype(jnp.bfloat16)
        total = jnp.dot(onehot, grows, preferred_element_type=jnp.float32)

        fresh = renorm(weighted + total)
        rounded = fresh.astype(jnp.bfloat16)
        scores = jnp.dot(rows, rounded.T, preferred_element_type=jnp.float32)
        local_best = jnp.max(scores, axis=1)
        top = jnp.max(lax.all_to_all(local_best.reshape(ncent, pdev), "cent", 0, 0, tiled=True), axis=0)
        values = points.astype(jnp.float32)
        scale = width * jnp.sqrt(jnp.mean(values * values, axis=1) + 1e-06)
        return (fresh, top / scale)

    return per_device


def solution(mesh):
    placed = (P(("dp", "cent"), None), P(("dp", "cent")), P("cent", None), P("cent"))
    return jax.shard_map(
        make_per_device(mesh.shape["cent"]),
        mesh=mesh,
        in_specs=placed,
        out_specs=(P("cent", None), P(("dp", "cent"))),
        check_vma=False,
    )
```

```python
import jax
import jax.numpy as jnp
from jax import lax
from jax.sharding import PartitionSpec as P


def renorm(merged):
    return merged * lax.rsqrt(jnp.mean(merged * merged, axis=1, keepdims=True) + 1e-05)


def make_per_device(ncent):
    def per_device(points, assign, centroids, counts):
        kdev = centroids.shape[0]
        pdev, width = points.shape
        first = lax.axis_index("cent") * kdev
        weighted = centroids * counts.astype(jnp.float32)[:, None]

        rows = lax.all_gather(points, "cent", axis=0, tiled=True)
        labels = lax.all_to_all(
            jnp.broadcast_to(assign[None], (ncent, pdev)), "cent", 0, 0, tiled=True
        ).reshape(-1)

        local = labels - first
        mine = (local >= 0) & (local < kdev)
        rank = jnp.cumsum(mine.astype(jnp.int32)) - 1
        pick = mine[None, :] & (rank[None, :] == jnp.arange(pdev, dtype=jnp.int32)[:, None])
        pick_rows, picked_label = lax.optimization_barrier(
            (pick.astype(jnp.bfloat16), jnp.sum(jnp.where(pick, local[None, :], 0), axis=1))
        )
        picked = jnp.dot(pick_rows, rows, preferred_element_type=jnp.float32)
        hi = (picked_label // 16).astype(jnp.bfloat16)
        lo = (picked_label % 16).astype(jnp.bfloat16)
        packed = jnp.concatenate(
            [picked.astype(jnp.bfloat16), hi[:, None], lo[:, None], jnp.zeros((pdev, 126), jnp.bfloat16)],
            axis=1,
        )

        gathered = lax.all_gather(packed, "dp", axis=0, tiled=True)
        grows = gathered[:, :width]
        glabel = gathered[:, width].astype(jnp.int32) * 16 + gathered[:, width + 1].astype(jnp.int32)
        onehot = (glabel[None, :] == jnp.arange(kdev, dtype=jnp.int32)[:, None]).astype(jnp.bfloat16)
        total = jnp.dot(onehot, grows, preferred_element_type=jnp.float32)

        fresh = renorm(weighted + total)
        rounded = fresh.astype(jnp.bfloat16)
        scores = jnp.dot(rows, rounded.T, preferred_element_type=jnp.float32)
        local_best = jnp.max(scores, axis=1)
        top = jnp.max(lax.all_to_all(local_best.reshape(ncent, pdev), "cent", 0, 0, tiled=True), axis=0)
        values = points.astype(jnp.float32)
        scale = width * jnp.sqrt(jnp.mean(values * values, axis=1) + 1e-06)
        return (fresh, top / scale)

    return per_device


def solution(mesh):
    placed = (P(("dp", "cent"), None), P(("dp", "cent")), P("cent", None), P("cent"))
    return jax.shard_map(
        make_per_device(mesh.shape["cent"]),
        mesh=mesh,
        in_specs=placed,
        out_specs=(P("cent", None), P(("dp", "cent"))),
        check_vma=False,
    )
```

```python
import jax
import jax.numpy as jnp
from jax import lax
from jax.experimental import pallas as pl
from jax.experimental.pallas import tpu as pltpu
from jax.sharding import PartitionSpec as P

SPAN = 8


def _take_rows_kernel(where_ref, rows_hbm, out_ref, slabs, sems):
    n = out_ref.shape[0]

    def copy(r):
        base = pl.multiple_of((where_ref[r] // SPAN) * SPAN, SPAN)
        return pltpu.make_async_copy(rows_hbm.at[pl.ds(base, SPAN)], slabs.at[r], sems.at[r])

    def start(r, carry):
        copy(r).start()
        return carry

    def finish(r, carry):
        copy(r).wait()
        return carry

    lax.fori_loop(0, n, start, 0)
    lax.fori_loop(0, n, finish, 0)
    offset = lax.broadcasted_iota(jnp.int32, (SPAN, out_ref.shape[1]), 0)
    for r in range(n):
        slab = slabs[r].astype(jnp.float32)
        keep = offset == where_ref[r] % SPAN
        out_ref[r : r + 1, :] = jnp.sum(jnp.where(keep, slab, 0.0), axis=0, keepdims=True)


def take_rows(rows, where):
    n, width = where.shape[0], rows.shape[1]
    return pl.pallas_call(
        _take_rows_kernel,
        out_shape=jax.ShapeDtypeStruct((n, width), jnp.float32),
        grid_spec=pltpu.PrefetchScalarGridSpec(
            num_scalar_prefetch=1,
            grid=(1,),
            in_specs=[pl.BlockSpec(memory_space=pl.ANY)],
            out_specs=pl.BlockSpec((n, width), lambda i, w: (0, 0)),
            scratch_shapes=[pltpu.VMEM((n, SPAN, width), rows.dtype), pltpu.SemaphoreType.DMA((n,))],
        ),
    )(where, rows)


def renorm(merged):
    return merged * lax.rsqrt(jnp.mean(merged * merged, axis=1, keepdims=True) + 1e-05)


def make_per_device(ncent):
    def per_device(points, assign, centroids, counts):
        kdev = centroids.shape[0]
        pdev, width = points.shape
        first = lax.axis_index("cent") * kdev
        weighted = centroids * counts.astype(jnp.float32)[:, None]

        rows = lax.all_gather(points, "cent", axis=0, tiled=True)
        labels = lax.all_to_all(
            jnp.broadcast_to(assign[None], (ncent, pdev)), "cent", 0, 0, tiled=True
        ).reshape(-1)

        local = labels - first
        mine = (local >= 0) & (local < kdev)
        rank = jnp.cumsum(mine.astype(jnp.int32)) - 1
        pick = mine[None, :] & (rank[None, :] == jnp.arange(pdev, dtype=jnp.int32)[:, None])
        where = jnp.sum(jnp.where(pick, jnp.arange(rows.shape[0], dtype=jnp.int32)[None, :], 0), axis=1)
        picked = take_rows(rows, where)
        picked_label = jnp.take(local, where, axis=0)
        hi = (picked_label // 16).astype(jnp.bfloat16)
        lo = (picked_label % 16).astype(jnp.bfloat16)
        packed = jnp.concatenate(
            [picked.astype(jnp.bfloat16), hi[:, None], lo[:, None], jnp.zeros((pdev, 126), jnp.bfloat16)],
            axis=1,
        )

        gathered = lax.all_gather(packed, "dp", axis=0, tiled=True)
        grows = gathered[:, :width]
        glabel = gathered[:, width].astype(jnp.int32) * 16 + gathered[:, width + 1].astype(jnp.int32)
        onehot = (glabel[None, :] == jnp.arange(kdev, dtype=jnp.int32)[:, None]).astype(jnp.bfloat16)
        total = jnp.dot(onehot, grows, preferred_element_type=jnp.float32)

        fresh = renorm(weighted + total)
        rounded = fresh.astype(jnp.bfloat16)
        scores = jnp.dot(rows, rounded.T, preferred_element_type=jnp.float32)
        local_best = jnp.max(scores, axis=1)
        top = jnp.max(lax.all_to_all(local_best.reshape(ncent, pdev), "cent", 0, 0, tiled=True), axis=0)
        values = points.astype(jnp.float32)
        scale = width * jnp.sqrt(jnp.mean(values * values, axis=1) + 1e-06)
        return (fresh, top / scale)

    return per_device


def solution(mesh):
    placed = (P(("dp", "cent"), None), P(("dp", "cent")), P("cent", None), P("cent"))
    return jax.shard_map(
        make_per_device(mesh.shape["cent"]),
        mesh=mesh,
        in_specs=placed,
        out_specs=(P("cent", None), P(("dp", "cent"))),
        check_vma=False,
    )
```

```python
import jax
import jax.numpy as jnp
from jax import lax
from jax.experimental import pallas as pl
from jax.experimental.pallas import tpu as pltpu
from jax.sharding import PartitionSpec as P

BLOCK = 512


def _best_kernel(cent_ref, rows_ref, out_ref):
    scores = lax.dot_general(
        cent_ref[...], rows_ref[...], (((1,), (1,)), ((), ())), preferred_element_type=jnp.float32
    )
    out_ref[...] = jnp.max(scores, axis=0, keepdims=True)


def best_scores(rows, rounded):
    n, width = rows.shape
    k = rounded.shape[0]
    return pl.pallas_call(
        _best_kernel,
        out_shape=jax.ShapeDtypeStruct((1, n), jnp.float32),
        grid=(n // BLOCK,),
        in_specs=[
            pl.BlockSpec((k, width), lambda i: (0, 0)),
            pl.BlockSpec((BLOCK, width), lambda i: (i, 0)),
        ],
        out_specs=pl.BlockSpec((1, BLOCK), lambda i: (0, i)),
    )(rounded, rows).reshape(n)


def renorm(merged):
    return merged * lax.rsqrt(jnp.mean(merged * merged, axis=1, keepdims=True) + 1e-05)


def make_per_device(ncent):
    def per_device(points, assign, centroids, counts):
        kdev = centroids.shape[0]
        pdev, width = points.shape
        first = lax.axis_index("cent") * kdev
        weighted = centroids * counts.astype(jnp.float32)[:, None]

        rows = lax.all_gather(points, "cent", axis=0, tiled=True)
        labels = lax.all_to_all(
            jnp.broadcast_to(assign[None], (ncent, pdev)), "cent", 0, 0, tiled=True
        ).reshape(-1)

        local = labels - first
        mine = (local >= 0) & (local < kdev)
        rank = jnp.cumsum(mine.astype(jnp.int32)) - 1
        pick = mine[None, :] & (rank[None, :] == jnp.arange(pdev, dtype=jnp.int32)[:, None])
        where = jnp.sum(jnp.where(pick, jnp.arange(rows.shape[0], dtype=jnp.int32)[None, :], 0), axis=1)
        picked = jnp.take(rows, where, axis=0)
        picked_label = jnp.take(local, where, axis=0)
        hi = (picked_label // 16).astype(jnp.bfloat16)
        lo = (picked_label % 16).astype(jnp.bfloat16)
        packed = jnp.concatenate(
            [picked.astype(jnp.bfloat16), hi[:, None], lo[:, None], jnp.zeros((pdev, 126), jnp.bfloat16)],
            axis=1,
        )

        gathered = lax.all_gather(packed, "dp", axis=0, tiled=True)
        grows = gathered[:, :width]
        glabel = gathered[:, width].astype(jnp.int32) * 16 + gathered[:, width + 1].astype(jnp.int32)
        onehot = (glabel[None, :] == jnp.arange(kdev, dtype=jnp.int32)[:, None]).astype(jnp.bfloat16)
        total = jnp.dot(onehot, grows, preferred_element_type=jnp.float32)

        fresh = renorm(weighted + total)
        rounded = fresh.astype(jnp.bfloat16)
        local_best = best_scores(rows, rounded)
        top = jnp.max(lax.all_to_all(local_best.reshape(ncent, pdev), "cent", 0, 0, tiled=True), axis=0)
        values = points.astype(jnp.float32)
        scale = width * jnp.sqrt(jnp.mean(values * values, axis=1) + 1e-06)
        return (fresh, top / scale)

    return per_device


def solution(mesh):
    placed = (P(("dp", "cent"), None), P(("dp", "cent")), P("cent", None), P("cent"))
    return jax.shard_map(
        make_per_device(mesh.shape["cent"]),
        mesh=mesh,
        in_specs=placed,
        out_specs=(P("cent", None), P(("dp", "cent"))),
        check_vma=False,
    )
```

```python
import jax
import jax.numpy as jnp
from jax import lax
from jax.sharding import PartitionSpec as P


def renorm(merged):
    return merged * lax.rsqrt(jnp.mean(merged * merged, axis=1, keepdims=True) + 1e-05)


def make_per_device(ncent):
    def per_device(points, assign, centroids, counts):
        kdev = centroids.shape[0]
        pdev, width = points.shape
        first = lax.axis_index("cent") * kdev
        weighted = centroids * counts.astype(jnp.float32)[:, None]

        rows = lax.all_gather(points, "cent", axis=0, tiled=True)
        labels = lax.all_to_all(
            jnp.broadcast_to(assign[None], (ncent, pdev)), "cent", 0, 0, tiled=True
        ).reshape(-1)

        local = labels - first
        mine = (local >= 0) & (local < kdev)
        rank = jnp.cumsum(mine.astype(jnp.int32)) - 1
        pick = mine[None, :] & (rank[None, :] == jnp.arange(pdev, dtype=jnp.int32)[:, None])
        where = jnp.sum(jnp.where(pick, jnp.arange(rows.shape[0], dtype=jnp.int32)[None, :], 0), axis=1)
        picked = jnp.take(rows, where, axis=0)
        picked_label = jnp.take(local, where, axis=0)
        hi = (picked_label // 16).astype(jnp.bfloat16)
        lo = (picked_label % 16).astype(jnp.bfloat16)
        packed = jnp.concatenate(
            [picked.astype(jnp.bfloat16), hi[:, None], lo[:, None], jnp.zeros((pdev, 126), jnp.bfloat16)],
            axis=1,
        )

        gathered = lax.all_gather(packed, "dp", axis=0, tiled=True)
        grows = gathered[:, :width]
        glabel = gathered[:, width].astype(jnp.int32) * 16 + gathered[:, width + 1].astype(jnp.int32)
        onehot = (glabel[None, :] == jnp.arange(kdev, dtype=jnp.int32)[:, None]).astype(jnp.bfloat16)
        total = jnp.dot(onehot, grows, preferred_element_type=jnp.float32)

        fresh = renorm(weighted + total)
        rounded = fresh.astype(jnp.bfloat16)
        scores = jnp.dot(rows, rounded.T, preferred_element_type=jnp.float32)
        local_best = jnp.max(scores.reshape(ncent, pdev, kdev), axis=2)
        received = lax.all_to_all(local_best, "cent", 0, 0, tiled=True)
        values = points.astype(jnp.float32)
        scale = width * jnp.sqrt(jnp.mean(values * values, axis=1) + 1e-06)
        return (fresh, jnp.max(received / scale[None, :], axis=0))

    return per_device


def solution(mesh):
    placed = (P(("dp", "cent"), None), P(("dp", "cent")), P("cent", None), P("cent"))
    return jax.shard_map(
        make_per_device(mesh.shape["cent"]),
        mesh=mesh,
        in_specs=placed,
        out_specs=(P("cent", None), P(("dp", "cent"))),
        check_vma=False,
    )
```

```python
import jax
import jax.numpy as jnp
from jax import lax
from jax.experimental import pallas as pl
from jax.experimental.pallas import tpu as pltpu
from jax.sharding import PartitionSpec as P

BLOCK = 1024


def _best_kernel(rows_ref, cent_t_ref, out_ref):
    scores = jnp.dot(rows_ref[...], cent_t_ref[...], preferred_element_type=jnp.float32)
    out_ref[...] = jnp.max(scores, axis=1, keepdims=True)


def best_scores(rows, cent_t):
    n, width = rows.shape
    k = cent_t.shape[1]
    return pl.pallas_call(
        _best_kernel,
        out_shape=jax.ShapeDtypeStruct((n, 1), jnp.float32),
        grid=(n // BLOCK,),
        in_specs=[
            pl.BlockSpec((BLOCK, width), lambda i: (i, 0)),
            pl.BlockSpec((width, k), lambda i: (0, 0)),
        ],
        out_specs=pl.BlockSpec((BLOCK, 1), lambda i: (i, 0)),
    )(rows, cent_t)


def renorm(merged):
    return merged * lax.rsqrt(jnp.mean(merged * merged, axis=1, keepdims=True) + 1e-05)


def make_per_device(ncent):
    def per_device(points, assign, centroids, counts):
        kdev = centroids.shape[0]
        pdev, width = points.shape
        first = lax.axis_index("cent") * kdev
        weighted = centroids * counts.astype(jnp.float32)[:, None]

        rows = lax.all_gather(points, "cent", axis=0, tiled=True)
        labels = lax.all_to_all(
            jnp.broadcast_to(assign[None], (ncent, pdev)), "cent", 0, 0, tiled=True
        ).reshape(-1)

        local = labels - first
        mine = (local >= 0) & (local < kdev)
        rank = jnp.cumsum(mine.astype(jnp.int32)) - 1
        pick = mine[None, :] & (rank[None, :] == jnp.arange(pdev, dtype=jnp.int32)[:, None])
        where = jnp.sum(jnp.where(pick, jnp.arange(rows.shape[0], dtype=jnp.int32)[None, :], 0), axis=1)
        picked = jnp.take(rows, where, axis=0)
        picked_label = jnp.take(local, where, axis=0)
        hi = (picked_label // 16).astype(jnp.bfloat16)
        lo = (picked_label % 16).astype(jnp.bfloat16)
        packed = jnp.concatenate(
            [picked.astype(jnp.bfloat16), hi[:, None], lo[:, None], jnp.zeros((pdev, 126), jnp.bfloat16)],
            axis=1,
        )

        gathered = lax.all_gather(packed, "dp", axis=0, tiled=True)
        grows = gathered[:, :width]
        glabel = gathered[:, width].astype(jnp.int32) * 16 + gathered[:, width + 1].astype(jnp.int32)
        onehot = (glabel[None, :] == jnp.arange(kdev, dtype=jnp.int32)[:, None]).astype(jnp.bfloat16)
        total = jnp.dot(onehot, grows, preferred_element_type=jnp.float32)

        fresh = renorm(weighted + total)
        rounded = fresh.astype(jnp.bfloat16)
        local_best = best_scores(rows, rounded.T).reshape(ncent, pdev)
        received = lax.all_to_all(local_best, "cent", 0, 0, tiled=True)
        values = points.astype(jnp.float32)
        scale = width * jnp.sqrt(jnp.mean(values * values, axis=1) + 1e-06)
        return (fresh, jnp.max(received / scale[None, :], axis=0))

    return per_device


def solution(mesh):
    placed = (P(("dp", "cent"), None), P(("dp", "cent")), P("cent", None), P("cent"))
    return jax.shard_map(
        make_per_device(mesh.shape["cent"]),
        mesh=mesh,
        in_specs=placed,
        out_specs=(P("cent", None), P(("dp", "cent"))),
        check_vma=False,
    )
```
